256 devices in a mesh: row: 8 (over x, core), col: 32 (over z, y).
Axes of the slice: x: 4, y: 4, z: 8, core: 2. Of those that a mesh axis runs over, the one named last changes fastest.
Arguments:
- row_points: bfloat16 [512, 64, 256], P('row'), may hold values from -25.5 to 25.5
- col_points: bfloat16 [128, 64, 256], P('col'), may hold values from -25.5 to 25.5
- block_lists: int32 [512, 16], P('row'), may hold values from 0 to 127, as said below
Outputs:
- row_potential: float32 [512, 256], P('row')
- col_potential: float32 [128, 256], P('col')
The draws below stay inside these ranges and needn't reach their ends.
Inputs may be any that keep to these rules, and one draw needn't show every extreme that they name: `block_lists`: the 16 column blocks of a row block are distinct. Among the row blocks of one index of row, at most 64 list entries name column blocks of one index of col, and exactly 64 for some index of col. Every column block is named by some row block of every index of row.
All inputs are finite; a program needn't handle non-finite values.
Results may differ from the reference program's by a relative error of at most 0.0003.
Values sent between devices are 32-bit elements; how exact they have to be, the bound alone decides.
No kernel may reach another device: no remote copies, remote signals or barrier semaphores. Data moves between devices by JAX's collectives and lax.ppermute only.
A program may use at most 64 MiB of HBM per device.

```python
import math
import jax
import jax.numpy as jnp
from jax import lax

BLOCK = 256
DIM = 64
LIST = 16
ITERS = 4
PAIR_MEAN = 32
COL_BLOCKS_DEV = 4
ROW_BLOCKS_DEV = 64
ROW_BLOCKS = 512
COL_BLOCKS = 128
N_ROW = 8
N_COL = 32


def point_cloud(key, blocks):
    subkeys = jax.random.split(key, 1)
    full_shape = (blocks, DIM, BLOCK)
    values = jnp.clip(jax.random.normal(subkeys[0], full_shape, jnp.float32), -4.0, 4.0)
    return values.astype(jnp.bfloat16)


def draw_row_points(key, part):
    return point_cloud(jax.random.fold_in(key, 11), ROW_BLOCKS)


def draw_col_points(key, part):
    return point_cloud(jax.random.fold_in(key, 23), COL_BLOCKS)


def shard_lists(shard_key):
    subkeys = jax.random.split(shard_key, 3)
    shuffle = jax.random.permutation(subkeys[0], N_COL)
    rank_list = jnp.arange(N_COL, dtype=jnp.int32)
    half_mean = PAIR_MEAN // 2
    spreads = jax.random.randint(subkeys[1], (N_COL,), 0, half_mean - COL_BLOCKS_DEV + 1, dtype=jnp.int32)
    offset_rank = rank_list - 3
    pair_index = jnp.maximum(offset_rank, 0) // 2
    sign_vals = jnp.where(offset_rank % 2 == 0, 1, -1).astype(jnp.int32)
    has_partner = (offset_rank % 2 == 1) | (rank_list + 1 < N_COL)
    paired = sign_vals * spreads[pair_index] * has_partner.astype(jnp.int32)
    adjust = jnp.where(rank_list == 0, PAIR_MEAN, jnp.where(rank_list < 3, -half_mean, paired)).astype(jnp.int32)
    counts = jnp.zeros((N_COL,), jnp.int32).at[shuffle].set(PAIR_MEAN + adjust)
    run_ends = jnp.cumsum(counts)
    starts = run_ends - counts
    positions = jnp.arange(LIST * ROW_BLOCKS_DEV, dtype=jnp.int32)
    device = jnp.sum((run_ends[None, :] <= positions[:, None]).astype(jnp.int32), axis=1)
    within = positions - starts[device]
    offsets = jax.random.randint(subkeys[2], (N_COL,), 0, COL_BLOCKS_DEV, dtype=jnp.int32)
    local_id = (offsets[device] + within + within // ROW_BLOCKS_DEV) % COL_BLOCKS_DEV
    block_ids = device * COL_BLOCKS_DEV + local_id
    return block_ids.reshape(LIST, ROW_BLOCKS_DEV).T


def draw_block_lists(key, part):
    shard_keys = jax.random.split(jax.random.fold_in(key, 37), N_ROW)
    return jax.vmap(shard_lists)(shard_keys).reshape(ROW_BLOCKS, LIST).astype(jnp.int32)


def setup_inputs(seed: int = 0) -> dict:
    splits = jax.random.split(jax.random.key(seed), 4)
    return {
        "row_points": draw_row_points(jax.random.fold_in(splits[3], 71), 0),
        "col_points": draw_col_points(jax.random.fold_in(splits[3], 71), 0),
        "block_lists": draw_block_lists(jax.random.fold_in(splits[3], 71), 0),
    }


eps_reg = 0.05
neg_big = -1.0e30


def cost_tiles(row_tile, row_norm, col_tiles, col_norms):
    inner_prod = jnp.einsum("dp,kdq->kpq", row_tile.astype(jnp.float32), col_tiles.astype(jnp.float32), precision=lax.Precision.HIGHEST)
    return (row_norm[None, :, None] + col_norms[:, None, :] - 2.0 * inner_prod) / DIM


def reference(row_points, col_points, block_lists):
    row_norms = jnp.sum(jnp.square(row_points.astype(jnp.float32)), axis=1)
    col_norms = jnp.sum(jnp.square(col_points.astype(jnp.float32)), axis=1)
    row_mass = -math.log(ROW_BLOCKS * BLOCK)
    col_mass = -math.log(COL_BLOCKS * BLOCK)
    flat_ids = block_lists.reshape(-1).astype(jnp.int32)
    col_potential = jnp.zeros((COL_BLOCKS, BLOCK), jnp.float32)
    row_potential = jnp.zeros((ROW_BLOCKS, BLOCK), jnp.float32)
    for sweep in range(ITERS):
        def row_update(members):
            row_tile, row_norm, listed = members
            tiles = cost_tiles(row_tile, row_norm, col_points[listed], col_norms[listed])
            scores = (col_potential[listed][:, None, :] - tiles) / eps_reg
            peak_vals = jnp.max(scores, axis=(0, 2))
            totals = jnp.sum(jnp.exp(scores - peak_vals[None, :, None]), axis=(0, 2))
            return eps_reg * (row_mass - (peak_vals + jnp.log(totals)))

        row_potential = lax.map(row_update, (row_points, row_norms, block_lists))

        def col_partials(members):
            row_tile, row_norm, row_pot, listed = members
            tiles = cost_tiles(row_tile, row_norm, col_points[listed], col_norms[listed])
            scores = (row_pot[None, :, None] - tiles) / eps_reg
            peak_vals = jnp.max(scores, axis=1)
            totals = jnp.sum(jnp.exp(scores - peak_vals[:, None, :]), axis=1)
            return peak_vals, totals

        peak_parts, partial_sums = lax.map(col_partials, (row_points, row_norms, row_potential, block_lists))
        peak_parts = peak_parts.reshape(-1, BLOCK)
        partial_sums = partial_sums.reshape(-1, BLOCK)
        block_peak = jnp.full((COL_BLOCKS, BLOCK), neg_big, jnp.float32).at[flat_ids].max(peak_parts)
        scaled = partial_sums * jnp.exp(peak_parts - block_peak[flat_ids])
        block_sum = jnp.zeros((COL_BLOCKS, BLOCK), jnp.float32).at[flat_ids].add(scaled)
        col_potential = eps_reg * (col_mass - (block_peak + jnp.log(block_sum)))
    return row_potential, col_potential
```

```python
import math

import jax
import jax.numpy as jnp
from jax import lax
from jax.sharding import PartitionSpec as P

DIM = 64
ITERS = 4
CAPACITY = 64


eps_reg = 0.05
neg_big = -1e30
group_slots = 8


def tile_partials(
    row_points, col_points, row_norms, col_norms, row_index, col_index, biases, over_columns
):
    row_tiles = row_points[row_index]
    col_tiles = col_points[col_index]
    inner_prod = jnp.einsum(
        "sdp,sdq->spq", row_tiles, col_tiles, preferred_element_type=jnp.float32
    )
    cost_tile = (
        row_norms[row_index][:, :, None] + col_norms[col_index][:, None, :] - 2.0 * inner_prod
    ) / DIM
    if over_columns:
        scores = (biases[:, None, :] - cost_tile) / eps_reg
        reduce_axis = 2
    else:
        scores = (biases[:, :, None] - cost_tile) / eps_reg
        reduce_axis = 1
    peak_vals = jnp.max(scores, axis=reduce_axis)
    totals = jnp.sum(jnp.exp(scores - jnp.expand_dims(peak_vals, reduce_axis)), axis=reduce_axis)
    return (peak_vals, totals)


def slot_partials(
    row_points, col_points, row_norms, col_norms, row_slot, col_slot, biases, over_columns
):
    groups = row_slot.shape[0] // group_slots
    block_size = row_points.shape[2]

    def one_group(members):
        return tile_partials(
            row_points,
            col_points,
            row_norms,
            col_norms,
            members[0],
            members[1],
            members[2],
            over_columns,
        )

    peak_parts, sum_parts = lax.map(
        one_group,
        (
            row_slot.reshape(groups, group_slots),
            col_slot.reshape(groups, group_slots),
            biases.reshape(groups, group_slots, block_size),
        ),
    )
    return (peak_parts.reshape(-1, block_size), sum_parts.reshape(-1, block_size))


def block_combine(peak_parts, sum_parts, members, slot_block, usable):
    block_peak = jnp.max(jnp.where(members[:, :, None], peak_parts[None, :, :], neg_big), axis=1)
    scale = jnp.where(usable[:, None], jnp.exp(peak_parts - block_peak[slot_block]), 0.0)
    block_sum = jnp.dot(
        members.astype(jnp.float32), sum_parts * scale, precision=lax.Precision.HIGHEST
    )
    return (block_peak, block_sum)


def lse_allreduce(peak_vals, totals, axis):
    size = lax.axis_size(axis)
    if size & (size - 1):
        whole_peak = lax.pmax(peak_vals, axis)
        whole_sum = lax.psum(totals * jnp.exp(peak_vals - whole_peak), axis)
        return (whole_peak, whole_sum)
    here = lax.axis_index(axis)
    pair = jnp.stack([peak_vals, totals])
    step = 1
    while step < size:
        other = lax.ppermute(pair, axis, [(i, i ^ step) for i in range(size)])
        low_side = (here // step) % 2 == 0
        lo = jnp.where(low_side, pair, other)
        hi = jnp.where(low_side, other, pair)
        top = jnp.maximum(lo[0], hi[0])
        total = lo[1] * jnp.exp(lo[0] - top) + hi[1] * jnp.exp(hi[0] - top)
        pair = jnp.stack([top, total])
        step *= 2
    return (pair[0], pair[1])


def potential_from(peak_vals, totals, log_mass):
    return eps_reg * (log_mass - (peak_vals + jnp.log(totals)))


def body(row_points, col_points, block_lists):
    row_blocks_here = row_points.shape[0]
    col_blocks_here = col_points.shape[0]
    block_size = row_points.shape[2]
    row_mass = -math.log(lax.axis_size("row") * row_blocks_here * block_size)
    col_mass = -math.log(lax.axis_size("col") * col_blocks_here * block_size)
    row_norms = jnp.sum(jnp.square(row_points.astype(jnp.float32)), axis=1)
    col_norms = jnp.sum(jnp.square(col_points.astype(jnp.float32)), axis=1)
    owned = (block_lists // col_blocks_here == lax.axis_index("col")).reshape(-1)
    entry_rank = jnp.cumsum(owned.astype(jnp.int32)) - 1
    slot_list = jnp.arange(CAPACITY, dtype=jnp.int32)
    picked = owned[None, :] & (entry_rank[None, :] == slot_list[:, None])
    entries = jnp.arange(owned.shape[0], dtype=jnp.int32)
    entry_of_slot = jnp.sum(jnp.where(picked, entries[None, :], 0), axis=1)
    usable = jnp.any(picked, axis=1)
    row_slot = entry_of_slot // block_lists.shape[1]
    col_slot = block_lists.reshape(-1)[entry_of_slot] % col_blocks_here
    row_members = (row_slot[None, :] == jnp.arange(row_blocks_here)[:, None]) & usable[None, :]
    col_members = (col_slot[None, :] == jnp.arange(col_blocks_here)[:, None]) & usable[None, :]
    col_potential = jnp.zeros((col_blocks_here, block_size), jnp.float32)
    row_potential = jnp.zeros((row_blocks_here, block_size), jnp.float32)
    for sweep in range(ITERS):
        peak_parts, sum_parts = slot_partials(
            row_points,
            col_points,
            row_norms,
            col_norms,
            row_slot,
            col_slot,
            col_potential[col_slot],
            True,
        )
        block_peak, block_sum = block_combine(peak_parts, sum_parts, row_members, row_slot, usable)
        whole_peak, whole_sum = lse_allreduce(block_peak, block_sum, "col")
        row_potential = potential_from(whole_peak, whole_sum, row_mass)
        peak_parts, sum_parts = slot_partials(
            row_points,
            col_points,
            row_norms,
            col_norms,
            row_slot,
            col_slot,
            row_potential[row_slot],
            False,
        )
        block_peak, block_sum = block_combine(peak_parts, sum_parts, col_members, col_slot, usable)
        whole_peak, whole_sum = lse_allreduce(block_peak, block_sum, "row")
        col_potential = potential_from(whole_peak, whole_sum, col_mass)
    return (row_potential, col_potential)


def solution(mesh):
    placed = (P("row", None, None), P("col", None, None), P("row", None))
    return jax.shard_map(
        body,
        mesh=mesh,
        in_specs=placed,
        out_specs=(P("row", None), P("col", None)),
        check_vma=False,
    )
```

```python
import math

import jax
import jax.numpy as jnp
from jax import lax
from jax.experimental import pallas as pl
from jax.experimental.pallas import tpu as pltpu
from jax.sharding import PartitionSpec as P

DIM = 64
ITERS = 4
CAPACITY = 64
AUG = 128


eps_reg = 0.05
neg_big = -1e30
ip_scale = 2.0 / (DIM * eps_reg)


def slot_kernel(lhs_slot, rhs_slot, lhs_ref, rhs_ref, peak_ref, sum_ref):
    def one_slot(k, carry):
        tile = jnp.dot(
            lhs_ref[lhs_slot[k]], rhs_ref[rhs_slot[k]], preferred_element_type=jnp.float32
        )
        scores = tile * ip_scale
        peak = jnp.max(scores, axis=0, keepdims=True)
        peak_ref[k] = peak
        sum_ref[k] = jnp.sum(jnp.exp(scores - peak), axis=0, keepdims=True)
        return carry

    lax.fori_loop(0, lhs_slot.shape[0], one_slot, 0)


def slot_partials(lhs_slot, rhs_slot, lhs, rhs):
    slots = lhs_slot.shape[0]
    block_size = rhs.shape[2]
    part = jax.ShapeDtypeStruct((slots, 1, block_size), jnp.float32)
    smem = pl.BlockSpec(memory_space=pltpu.SMEM)
    vmem = pl.BlockSpec(memory_space=pltpu.VMEM)
    peak_parts, sum_parts = pl.pallas_call(
        slot_kernel,
        out_shape=(part, part),
        in_specs=[smem, smem, vmem, vmem],
        out_specs=(vmem, vmem),
        cost_estimate=pl.CostEstimate(
            flops=2 * slots * lhs.shape[1] * lhs.shape[2] * block_size,
            transcendentals=slots * lhs.shape[1] * block_size,
            bytes_accessed=(lhs.size + rhs.size) * 2 + 2 * slots * block_size * 4,
        ),
    )(lhs_slot, rhs_slot, lhs, rhs)
    return (peak_parts.reshape(slots, block_size), sum_parts.reshape(slots, block_size))


def bias_columns(bias):
    scaled = bias / ip_scale
    hi = lax.reduce_precision(scaled, exponent_bits=8, mantissa_bits=7)
    rest = scaled - hi
    mid = lax.reduce_precision(rest, exponent_bits=8, mantissa_bits=7)
    lo = rest - mid
    return jnp.stack([hi, mid, lo], axis=-1).astype(jnp.bfloat16)


def with_bias(points_t, bias):
    blocks, block_size, dim = points_t.shape
    pad = jnp.zeros((blocks, block_size, AUG - dim - 3), jnp.bfloat16)
    return jnp.concatenate([points_t, bias_columns(bias), pad], axis=-1)


def with_ones(points):
    blocks, dim, block_size = points.shape
    ones = jnp.ones((blocks, 3, block_size), jnp.bfloat16)
    pad = jnp.zeros((blocks, AUG - dim - 3, block_size), jnp.bfloat16)
    return jnp.concatenate([points, ones, pad], axis=1)


def block_combine(peak_parts, sum_parts, members, slot_block, usable):
    block_peak = jnp.max(jnp.where(members[:, :, None], peak_parts[None, :, :], neg_big), axis=1)
    scale = jnp.where(usable[:, None], jnp.exp(peak_parts - block_peak[slot_block]), 0.0)
    block_sum = jnp.dot(
        members.astype(jnp.float32), sum_parts * scale, precision=lax.Precision.HIGHEST
    )
    return (block_peak, block_sum)


def lse_allreduce(peak_vals, totals, axis):
    size = lax.axis_size(axis)
    if size & (size - 1):
        whole_peak = lax.pmax(peak_vals, axis)
        whole_sum = lax.psum(totals * jnp.exp(peak_vals - whole_peak), axis)
        return (whole_peak, whole_sum)
    here = lax.axis_index(axis)
    pair = jnp.stack([peak_vals, totals])
    step = 1
    while step < size:
        other = lax.ppermute(pair, axis, [(i, i ^ step) for i in range(size)])
        low_side = (here // step) % 2 == 0
        lo = jnp.where(low_side, pair, other)
        hi = jnp.where(low_side, other, pair)
        top = jnp.maximum(lo[0], hi[0])
        total = lo[1] * jnp.exp(lo[0] - top) + hi[1] * jnp.exp(hi[0] - top)
        pair = jnp.stack([top, total])
        step *= 2
    return (pair[0], pair[1])


def potential_from(peak_vals, totals, log_mass):
    return eps_reg * (log_mass - (peak_vals + jnp.log(totals)))


def body(row_points, col_points, block_lists):
    row_blocks_here = row_points.shape[0]
    col_blocks_here = col_points.shape[0]
    block_size = row_points.shape[2]
    row_mass = -math.log(lax.axis_size("row") * row_blocks_here * block_size)
    col_mass = -math.log(lax.axis_size("col") * col_blocks_here * block_size)
    row_norms = jnp.sum(jnp.square(row_points.astype(jnp.float32)), axis=1)
    col_norms = jnp.sum(jnp.square(col_points.astype(jnp.float32)), axis=1)
    owned = (block_lists // col_blocks_here == lax.axis_index("col")).reshape(-1)
    entry_rank = jnp.cumsum(owned.astype(jnp.int32)) - 1
    slot_list = jnp.arange(CAPACITY, dtype=jnp.int32)
    picked = owned[None, :] & (entry_rank[None, :] == slot_list[:, None])
    entries = jnp.arange(owned.shape[0], dtype=jnp.int32)
    entry_of_slot = jnp.sum(jnp.where(picked, entries[None, :], 0), axis=1)
    usable = jnp.any(picked, axis=1)
    row_slot = entry_of_slot // block_lists.shape[1]
    col_slot = block_lists.reshape(-1)[entry_of_slot] % col_blocks_here
    row_members = (row_slot[None, :] == jnp.arange(row_blocks_here)[:, None]) & usable[None, :]
    col_members = (col_slot[None, :] == jnp.arange(col_blocks_here)[:, None]) & usable[None, :]
    row_t = jnp.swapaxes(row_points, 1, 2)
    col_t = jnp.swapaxes(col_points, 1, 2)
    row_ones = with_ones(row_points)
    col_ones = with_ones(col_points)
    row_own = -row_norms / (DIM * eps_reg)
    col_own = -col_norms / (DIM * eps_reg)
    def sweep(step, carry):
        row_potential, col_potential = carry
        col_bias = (col_potential - col_norms / DIM) / eps_reg
        peak_parts, sum_parts = slot_partials(
            col_slot, row_slot, with_bias(col_t, col_bias), row_ones
        )
        block_peak, block_sum = block_combine(peak_parts, sum_parts, row_members, row_slot, usable)
        whole_peak, whole_sum = lse_allreduce(block_peak + row_own, block_sum, "col")
        row_potential = potential_from(whole_peak, whole_sum, row_mass)
        row_bias = (row_potential - row_norms / DIM) / eps_reg
        peak_parts, sum_parts = slot_partials(
            row_slot, col_slot, with_bias(row_t, row_bias), col_ones
        )
        block_peak, block_sum = block_combine(peak_parts, sum_parts, col_members, col_slot, usable)
        whole_peak, whole_sum = lse_allreduce(block_peak + col_own, block_sum, "row")
        col_potential = potential_from(whole_peak, whole_sum, col_mass)
        return (row_potential, col_potential)

    start = (
        jnp.zeros((row_blocks_here, block_size), jnp.float32),
        jnp.zeros((col_blocks_here, block_size), jnp.float32),
    )
    row_potential, col_potential = lax.fori_loop(0, ITERS, sweep, start)
    return (row_potential, col_potential)


def solution(mesh):
    placed = (P("row", None, None), P("col", None, None), P("row", None))
    return jax.shard_map(
        body,
        mesh=mesh,
        in_specs=placed,
        out_specs=(P("row", None), P("col", None)),
        check_vma=False,
    )
```

```python
import math

import jax
import jax.numpy as jnp
from jax import lax
from jax.experimental import pallas as pl
from jax.experimental.pallas import tpu as pltpu
from jax.sharding import PartitionSpec as P

DIM = 64
ITERS = 4
CAPACITY = 64
LANES = 128


eps_reg = 0.05
neg_big = -1e30
ip_scale = 2.0 / (DIM * eps_reg)


def slot_kernel(lhs_slot, rhs_slot, lhs_ref, rhs_ref, bias_ref, peak_ref, sum_ref, spread_ref):
    lanes = spread_ref.shape[2]

    def spread(block, carry):
        row = jnp.broadcast_to(bias_ref[block], (lanes, bias_ref.shape[2]))
        spread_ref[block] = jnp.transpose(row)
        return carry

    lax.fori_loop(0, spread_ref.shape[0], spread, 0)

    def one_slot(k, carry):
        a = lhs_slot[k]
        tile = jnp.dot(lhs_ref[a], rhs_ref[rhs_slot[k]], preferred_element_type=jnp.float32)
        bias = spread_ref[a]
        bias = jnp.concatenate([bias] * (tile.shape[1] // lanes), axis=1)
        scores = tile * ip_scale + bias
        peak = jnp.max(scores, axis=0, keepdims=True)
        peak_ref[k] = peak
        sum_ref[k] = jnp.sum(jnp.exp(scores - peak), axis=0, keepdims=True)
        return carry

    lax.fori_loop(0, lhs_slot.shape[0], one_slot, 0)


def slot_partials(lhs_slot, rhs_slot, lhs, rhs, bias):
    slots = lhs_slot.shape[0]
    blocks, block_size, dim = lhs.shape
    part = jax.ShapeDtypeStruct((slots, 1, rhs.shape[2]), jnp.float32)
    smem = pl.BlockSpec(memory_space=pltpu.SMEM)
    vmem = pl.BlockSpec(memory_space=pltpu.VMEM)
    peak_parts, sum_parts = pl.pallas_call(
        slot_kernel,
        out_shape=(part, part),
        in_specs=[smem, smem, vmem, vmem, vmem],
        out_specs=(vmem, vmem),
        scratch_shapes=[pltpu.VMEM((blocks, block_size, LANES), jnp.float32)],
        cost_estimate=pl.CostEstimate(
            flops=2 * slots * block_size * dim * rhs.shape[2],
            transcendentals=slots * block_size * rhs.shape[2],
            bytes_accessed=(lhs.size + rhs.size) * 2 + 2 * slots * rhs.shape[2] * 4,
        ),
    )(lhs_slot, rhs_slot, lhs, rhs, bias.reshape(blocks, 1, block_size))
    return (peak_parts.reshape(slots, -1), sum_parts.reshape(slots, -1))


def block_combine(peak_parts, sum_parts, members, slot_block, usable):
    block_peak = jnp.max(jnp.where(members[:, :, None], peak_parts[None, :, :], neg_big), axis=1)
    scale = jnp.where(usable[:, None], jnp.exp(peak_parts - block_peak[slot_block]), 0.0)
    block_sum = jnp.dot(
        members.astype(jnp.float32), sum_parts * scale, precision=lax.Precision.HIGHEST
    )
    return (block_peak, block_sum)


def lse_allreduce(peak_vals, totals, axis):
    size = lax.axis_size(axis)
    if size & (size - 1):
        whole_peak = lax.pmax(peak_vals, axis)
        whole_sum = lax.psum(totals * jnp.exp(peak_vals - whole_peak), axis)
        return (whole_peak, whole_sum)
    here = lax.axis_index(axis)
    pair = jnp.stack([peak_vals, totals])
    step = 1
    while step < size:
        other = lax.ppermute(pair, axis, [(i, i ^ step) for i in range(size)])
        low_side = (here // step) % 2 == 0
        lo = jnp.where(low_side, pair, other)
        hi = jnp.where(low_side, other, pair)
        top = jnp.maximum(lo[0], hi[0])
        total = lo[1] * jnp.exp(lo[0] - top) + hi[1] * jnp.exp(hi[0] - top)
        pair = jnp.stack([top, total])
        step *= 2
    return (pair[0], pair[1])


def potential_from(peak_vals, totals, log_mass):
    return eps_reg * (log_mass - (peak_vals + jnp.log(totals)))


def body(row_points, col_points, block_lists):
    row_blocks_here = row_points.shape[0]
    col_blocks_here = col_points.shape[0]
    block_size = row_points.shape[2]
    row_mass = -math.log(lax.axis_size("row") * row_blocks_here * block_size)
    col_mass = -math.log(lax.axis_size("col") * col_blocks_here * block_size)
    row_norms = jnp.sum(jnp.square(row_points.astype(jnp.float32)), axis=1)
    col_norms = jnp.sum(jnp.square(col_points.astype(jnp.float32)), axis=1)
    owned = (block_lists // col_blocks_here == lax.axis_index("col")).reshape(-1)
    entry_rank = jnp.cumsum(owned.astype(jnp.int32)) - 1
    slot_list = jnp.arange(CAPACITY, dtype=jnp.int32)
    picked = owned[None, :] & (entry_rank[None, :] == slot_list[:, None])
    entries = jnp.arange(owned.shape[0], dtype=jnp.int32)
    entry_of_slot = jnp.sum(jnp.where(picked, entries[None, :], 0), axis=1)
    usable = jnp.any(picked, axis=1)
    row_slot = entry_of_slot // block_lists.shape[1]
    col_slot = block_lists.reshape(-1)[entry_of_slot] % col_blocks_here
    row_members = (row_slot[None, :] == jnp.arange(row_blocks_here)[:, None]) & usable[None, :]
    col_members = (col_slot[None, :] == jnp.arange(col_blocks_here)[:, None]) & usable[None, :]
    row_t = jnp.swapaxes(row_points, 1, 2)
    col_t = jnp.swapaxes(col_points, 1, 2)
    row_own = -row_norms / (DIM * eps_reg)
    col_own = -col_norms / (DIM * eps_reg)
    def sweep(step, carry):
        row_potential, col_potential = carry
        col_bias = (col_potential - col_norms / DIM) / eps_reg
        peak_parts, sum_parts = slot_partials(
            col_slot, row_slot, col_t, row_points, col_bias
        )
        block_peak, block_sum = block_combine(peak_parts, sum_parts, row_members, row_slot, usable)
        whole_peak, whole_sum = lse_allreduce(block_peak + row_own, block_sum, "col")
        row_potential = potential_from(whole_peak, whole_sum, row_mass)
        row_bias = (row_potential - row_norms / DIM) / eps_reg
        peak_parts, sum_parts = slot_partials(
            row_slot, col_slot, row_t, col_points, row_bias
        )
        block_peak, block_sum = block_combine(peak_parts, sum_parts, col_members, col_slot, usable)
        whole_peak, whole_sum = lse_allreduce(block_peak + col_own, block_sum, "row")
        col_potential = potential_from(whole_peak, whole_sum, col_mass)
        return (row_potential, col_potential)

    start = (
        jnp.zeros((row_blocks_here, block_size), jnp.float32),
        jnp.zeros((col_blocks_here, block_size), jnp.float32),
    )
    row_potential, col_potential = lax.fori_loop(0, ITERS, sweep, start)
    return (row_potential, col_potential)


def solution(mesh):
    placed = (P("row", None, None), P("col", None, None), P("row", None))
    return jax.shard_map(
        body,
        mesh=mesh,
        in_specs=placed,
        out_specs=(P("row", None), P("col", None)),
        check_vma=False,
    )
```

```python
import math

import jax
import jax.numpy as jnp
from jax import lax
from jax.experimental import pallas as pl
from jax.experimental.pallas import tpu as pltpu
from jax.sharding import PartitionSpec as P

DIM = 64
ITERS = 4
CAPACITY = 64
LANES = 128


eps_reg = 0.05
neg_big = -1e30
ip_scale = 2.0 / (DIM * eps_reg)


def slot_kernel(lhs_slot, rhs_slot, lhs_ref, rhs_ref, bias_ref, peak_ref, sum_ref, spread_ref):
    lanes = spread_ref.shape[2]

    def spread(block, carry):
        row = jnp.broadcast_to(bias_ref[block], (lanes, bias_ref.shape[2]))
        spread_ref[block] = jnp.transpose(row)
        return carry

    lax.fori_loop(0, spread_ref.shape[0], spread, 0)

    def one_slot(k, carry):
        a = lhs_slot[k]
        tile = jnp.dot(lhs_ref[a], rhs_ref[rhs_slot[k]], preferred_element_type=jnp.float32)
        bias = spread_ref[a]
        bias = jnp.concatenate([bias] * (tile.shape[1] // lanes), axis=1)
        scores = tile * ip_scale + bias
        peak = jnp.max(scores, axis=0, keepdims=True)
        peak_ref[k] = peak
        sum_ref[k] = jnp.sum(jnp.exp(scores - peak), axis=0, keepdims=True)
        return carry

    lax.fori_loop(0, lhs_slot.shape[0], one_slot, 0)


def slot_partials(lhs_slot, rhs_slot, lhs, rhs, bias):
    slots = lhs_slot.shape[0]
    blocks, block_size, dim = lhs.shape
    part = jax.ShapeDtypeStruct((slots, 1, rhs.shape[2]), jnp.float32)
    smem = pl.BlockSpec(memory_space=pltpu.SMEM)
    vmem = pl.BlockSpec(memory_space=pltpu.VMEM)
    peak_parts, sum_parts = pl.pallas_call(
        slot_kernel,
        out_shape=(part, part),
        in_specs=[smem, smem, vmem, vmem, vmem],
        out_specs=(vmem, vmem),
        scratch_shapes=[pltpu.VMEM((blocks, block_size, LANES), jnp.float32)],
        cost_estimate=pl.CostEstimate(
            flops=2 * slots * block_size * dim * rhs.shape[2],
            transcendentals=slots * block_size * rhs.shape[2],
            bytes_accessed=(lhs.size + rhs.size) * 2 + 2 * slots * rhs.shape[2] * 4,
        ),
    )(lhs_slot, rhs_slot, lhs, rhs, bias.reshape(blocks, 1, block_size))
    return (peak_parts.reshape(slots, -1), sum_parts.reshape(slots, -1))


def block_combine(peak_parts, sum_parts, members, slot_block, usable):
    block_peak = jnp.max(jnp.where(members[:, :, None], peak_parts[None, :, :], neg_big), axis=1)
    scale = jnp.where(usable[:, None], jnp.exp(peak_parts - block_peak[slot_block]), 0.0)
    block_sum = jnp.dot(
        members.astype(jnp.float32), sum_parts * scale, precision=lax.Precision.HIGHEST
    )
    return (block_peak, block_sum)


def merge_pair(low, high):
    top = jnp.maximum(low[0], high[0])
    total = low[1] * jnp.exp(low[0] - top) + high[1] * jnp.exp(high[0] - top)
    return jnp.stack([top, total])


def round_bits(size, widest):
    bits = size.bit_length() - 1
    plan = []
    first = 0
    while first < bits:
        width = min(widest, bits - first)
        plan.append((first, width))
        first += width
    return plan


def lse_allreduce(peak_vals, totals, axis, widest):
    size = lax.axis_size(axis)
    if size & (size - 1):
        whole_peak = lax.pmax(peak_vals, axis)
        whole_sum = lax.psum(totals * jnp.exp(peak_vals - whole_peak), axis)
        return (whole_peak, whole_sum)
    here = lax.axis_index(axis)
    pair = jnp.stack([peak_vals, totals])
    for first, width in round_bits(size, widest):
        step = 1 << first
        held = {0: pair}
        for offset in range(1, 1 << width):
            shift = offset * step
            held[offset] = lax.ppermute(pair, axis, [(i, i ^ shift) for i in range(size)])
        for level in range(width):
            low_side = (here // (step << level)) % 2 == 0
            merged = {}
            for offset, value in held.items():
                if offset & (1 << level):
                    continue
                other = held[offset | (1 << level)]
                low = jnp.where(low_side, value, other)
                high = jnp.where(low_side, other, value)
                merged[offset] = merge_pair(low, high)
            held = merged
        pair = held[0]
    return (pair[0], pair[1])


def potential_from(peak_vals, totals, log_mass):
    return eps_reg * (log_mass - (peak_vals + jnp.log(totals)))


def body(row_points, col_points, block_lists):
    row_blocks_here = row_points.shape[0]
    col_blocks_here = col_points.shape[0]
    block_size = row_points.shape[2]
    row_mass = -math.log(lax.axis_size("row") * row_blocks_here * block_size)
    col_mass = -math.log(lax.axis_size("col") * col_blocks_here * block_size)
    row_norms = jnp.sum(jnp.square(row_points.astype(jnp.float32)), axis=1)
    col_norms = jnp.sum(jnp.square(col_points.astype(jnp.float32)), axis=1)
    owned = (block_lists // col_blocks_here == lax.axis_index("col")).reshape(-1)
    entry_rank = jnp.cumsum(owned.astype(jnp.int32)) - 1
    slot_list = jnp.arange(CAPACITY, dtype=jnp.int32)
    picked = owned[None, :] & (entry_rank[None, :] == slot_list[:, None])
    entries = jnp.arange(owned.shape[0], dtype=jnp.int32)
    entry_of_slot = jnp.sum(jnp.where(picked, entries[None, :], 0), axis=1)
    usable = jnp.any(picked, axis=1)
    row_slot = entry_of_slot // block_lists.shape[1]
    col_slot = block_lists.reshape(-1)[entry_of_slot] % col_blocks_here
    row_members = (row_slot[None, :] == jnp.arange(row_blocks_here)[:, None]) & usable[None, :]
    col_members = (col_slot[None, :] == jnp.arange(col_blocks_here)[:, None]) & usable[None, :]
    row_t = jnp.swapaxes(row_points, 1, 2)
    col_t = jnp.swapaxes(col_points, 1, 2)
    row_own = -row_norms / (DIM * eps_reg)
    col_own = -col_norms / (DIM * eps_reg)
    def sweep(step, carry):
        row_potential, col_potential = carry
        col_bias = (col_potential - col_norms / DIM) / eps_reg
        peak_parts, sum_parts = slot_partials(
            col_slot, row_slot, col_t, row_points, col_bias
        )
        block_peak, block_sum = block_combine(peak_parts, sum_parts, row_members, row_slot, usable)
        whole_peak, whole_sum = lse_allreduce(block_peak + row_own, block_sum, "col", 2)
        row_potential = potential_from(whole_peak, whole_sum, row_mass)
        row_bias = (row_potential - row_norms / DIM) / eps_reg
        peak_parts, sum_parts = slot_partials(
            row_slot, col_slot, row_t, col_points, row_bias
        )
        block_peak, block_sum = block_combine(peak_parts, sum_parts, col_members, col_slot, usable)
        whole_peak, whole_sum = lse_allreduce(block_peak + col_own, block_sum, "row", 3)
        col_potential = potential_from(whole_peak, whole_sum, col_mass)
        return (row_potential, col_potential)

    start = (
        jnp.zeros((row_blocks_here, block_size), jnp.float32),
        jnp.zeros((col_blocks_here, block_size), jnp.float32),
    )
    row_potential, col_potential = lax.fori_loop(0, ITERS, sweep, start)
    return (row_potential, col_potential)


def solution(mesh):
    placed = (P("row", None, None), P("col", None, None), P("row", None))
    return jax.shard_map(
        body,
        mesh=mesh,
        in_specs=placed,
        out_specs=(P("row", None), P("col", None)),
        check_vma=False,
    )
```

```python
import math

import jax
import jax.numpy as jnp
from jax import lax
from jax.experimental import pallas as pl
from jax.experimental.pallas import tpu as pltpu
from jax.sharding import PartitionSpec as P

DIM = 64
ITERS = 4
CAPACITY = 64
LANES = 128


eps_reg = 0.05
neg_big = -1e30
ip_scale = 2.0 / (DIM * eps_reg)


def slot_kernel(lhs_slot, rhs_slot, lhs_ref, rhs_ref, bias_ref, peak_ref, sum_ref, spread_ref):
    lanes = spread_ref.shape[2]

    def spread(block, carry):
        row = jnp.broadcast_to(bias_ref[block], (lanes, bias_ref.shape[2]))
        spread_ref[block] = jnp.transpose(row)
        return carry

    lax.fori_loop(0, spread_ref.shape[0], spread, 0)

    def one_slot(k, carry):
        a = lhs_slot[k]
        tile = jnp.dot(lhs_ref[a], rhs_ref[rhs_slot[k]], preferred_element_type=jnp.float32)
        bias = spread_ref[a]
        bias = jnp.concatenate([bias] * (tile.shape[1] // lanes), axis=1)
        scores = tile * ip_scale + bias
        peak = jnp.max(scores, axis=0, keepdims=True)
        peak_ref[k] = peak
        sum_ref[k] = jnp.sum(jnp.exp(scores - peak), axis=0, keepdims=True)
        return carry

    lax.fori_loop(0, lhs_slot.shape[0], one_slot, 0, unroll=2)


def slot_partials(lhs_slot, rhs_slot, lhs, rhs, bias):
    slots = lhs_slot.shape[0]
    blocks, block_size, dim = lhs.shape
    part = jax.ShapeDtypeStruct((slots, 1, rhs.shape[2]), jnp.float32)
    smem = pl.BlockSpec(memory_space=pltpu.SMEM)
    vmem = pl.BlockSpec(memory_space=pltpu.VMEM)
    peak_parts, sum_parts = pl.pallas_call(
        slot_kernel,
        out_shape=(part, part),
        in_specs=[smem, smem, vmem, vmem, vmem],
        out_specs=(vmem, vmem),
        scratch_shapes=[pltpu.VMEM((blocks, block_size, LANES), jnp.float32)],
        cost_estimate=pl.CostEstimate(
            flops=2 * slots * block_size * dim * rhs.shape[2],
            transcendentals=slots * block_size * rhs.shape[2],
            bytes_accessed=(lhs.size + rhs.size) * 2 + 2 * slots * rhs.shape[2] * 4,
        ),
    )(lhs_slot, rhs_slot, lhs, rhs, bias.reshape(blocks, 1, block_size))
    return (peak_parts.reshape(slots, -1), sum_parts.reshape(slots, -1))


def block_combine(peak_parts, sum_parts, members, slot_block, usable):
    block_peak = jnp.max(jnp.where(members[:, :, None], peak_parts[None, :, :], neg_big), axis=1)
    scale = jnp.where(usable[:, None], jnp.exp(peak_parts - block_peak[slot_block]), 0.0)
    block_sum = jnp.dot(
        members.astype(jnp.float32), sum_parts * scale, precision=lax.Precision.HIGHEST
    )
    return (block_peak, block_sum)


def merge_pair(low, high):
    top = jnp.maximum(low[0], high[0])
    total = low[1] * jnp.exp(low[0] - top) + high[1] * jnp.exp(high[0] - top)
    return jnp.stack([top, total])


def round_bits(size, widest):
    bits = size.bit_length() - 1
    plan = []
    first = 0
    while first < bits:
        width = min(widest, bits - first)
        plan.append((first, width))
        first += width
    return plan


def lse_allreduce(peak_vals, totals, axis, widest):
    size = lax.axis_size(axis)
    if size & (size - 1):
        whole_peak = lax.pmax(peak_vals, axis)
        whole_sum = lax.psum(totals * jnp.exp(peak_vals - whole_peak), axis)
        return (whole_peak, whole_sum)
    here = lax.axis_index(axis)
    pair = jnp.stack([peak_vals, totals])
    for first, width in round_bits(size, widest):
        step = 1 << first
        held = {0: pair}
        for offset in range(1, 1 << width):
            shift = offset * step
            held[offset] = lax.ppermute(pair, axis, [(i, i ^ shift) for i in range(size)])
        for level in range(width):
            low_side = (here // (step << level)) % 2 == 0
            merged = {}
            for offset, value in held.items():
                if offset & (1 << level):
                    continue
                other = held[offset | (1 << level)]
                low = jnp.where(low_side, value, other)
                high = jnp.where(low_side, other, value)
                merged[offset] = merge_pair(low, high)
            held = merged
        pair = held[0]
    return (pair[0], pair[1])


def potential_from(peak_vals, totals, log_mass):
    return eps_reg * (log_mass - (peak_vals + jnp.log(totals)))


def body(row_points, col_points, block_lists):
    row_blocks_here = row_points.shape[0]
    col_blocks_here = col_points.shape[0]
    block_size = row_points.shape[2]
    row_mass = -math.log(lax.axis_size("row") * row_blocks_here * block_size)
    col_mass = -math.log(lax.axis_size("col") * col_blocks_here * block_size)
    row_norms = jnp.sum(jnp.square(row_points.astype(jnp.float32)), axis=1)
    col_norms = jnp.sum(jnp.square(col_points.astype(jnp.float32)), axis=1)
    owned = (block_lists // col_blocks_here == lax.axis_index("col")).reshape(-1)
    entry_rank = jnp.cumsum(owned.astype(jnp.int32)) - 1
    slot_list = jnp.arange(CAPACITY, dtype=jnp.int32)
    picked = owned[None, :] & (entry_rank[None, :] == slot_list[:, None])
    entries = jnp.arange(owned.shape[0], dtype=jnp.int32)
    entry_of_slot = jnp.sum(jnp.where(picked, entries[None, :], 0), axis=1)
    usable = jnp.any(picked, axis=1)
    row_slot = entry_of_slot // block_lists.shape[1]
    col_slot = block_lists.reshape(-1)[entry_of_slot] % col_blocks_here
    row_members = (row_slot[None, :] == jnp.arange(row_blocks_here)[:, None]) & usable[None, :]
    col_members = (col_slot[None, :] == jnp.arange(col_blocks_here)[:, None]) & usable[None, :]
    row_t = jnp.swapaxes(row_points, 1, 2)
    col_t = jnp.swapaxes(col_points, 1, 2)
    row_own = -row_norms / (DIM * eps_reg)
    col_own = -col_norms / (DIM * eps_reg)
    def sweep(step, carry):
        row_potential, col_potential = carry
        col_bias = (col_potential - col_norms / DIM) / eps_reg
        peak_parts, sum_parts = slot_partials(
            col_slot, row_slot, col_t, row_points, col_bias
        )
        block_peak, block_sum = block_combine(peak_parts, sum_parts, row_members, row_slot, usable)
        whole_peak, whole_sum = lse_allreduce(block_peak + row_own, block_sum, "col", 2)
        row_potential = potential_from(whole_peak, whole_sum, row_mass)
        row_bias = (row_potential - row_norms / DIM) / eps_reg
        peak_parts, sum_parts = slot_partials(
            row_slot, col_slot, row_t, col_points, row_bias
        )
        block_peak, block_sum = block_combine(peak_parts, sum_parts, col_members, col_slot, usable)
        whole_peak, whole_sum = lse_allreduce(block_peak + col_own, block_sum, "row", 3)
        col_potential = potential_from(whole_peak, whole_sum, col_mass)
        return (row_potential, col_potential)

    start = (
        jnp.zeros((row_blocks_here, block_size), jnp.float32),
        jnp.zeros((col_blocks_here, block_size), jnp.float32),
    )
    row_potential, col_potential = lax.fori_loop(0, ITERS, sweep, start)
    return (row_potential, col_potential)


def solution(mesh):
    placed = (P("row", None, None), P("col", None, None), P("row", None))
    return jax.shard_map(
        body,
        mesh=mesh,
        in_specs=placed,
        out_specs=(P("row", None), P("col", None)),
        check_vma=False,
    )
```

```python
import math

import jax
import jax.numpy as jnp
from jax import lax
from jax.experimental import pallas as pl
from jax.experimental.pallas import tpu as pltpu
from jax.sharding import PartitionSpec as P

DIM = 64
ITERS = 4
CAPACITY = 64
LANES = 128


eps_reg = 0.05
neg_big = -1e30
ip_scale = 2.0 / (DIM * eps_reg)


def slot_kernel(lhs_slot, rhs_slot, lhs_ref, rhs_ref, bias_ref, peak_ref, sum_ref, spread_ref):
    lanes = spread_ref.shape[2]

    def spread(block, carry):
        row = jnp.broadcast_to(bias_ref[block], (lanes, bias_ref.shape[2]))
        spread_ref[block] = jnp.transpose(row)
        return carry

    lax.fori_loop(0, spread_ref.shape[0], spread, 0, unroll=4)

    def one_slot(k, carry):
        a = lhs_slot[k]
        tile = jnp.dot(lhs_ref[a], rhs_ref[rhs_slot[k]], preferred_element_type=jnp.float32)
        bias = spread_ref[a]
        bias = jnp.concatenate([bias] * (tile.shape[1] // lanes), axis=1)
        scores = tile * ip_scale + bias
        peak = jnp.max(scores, axis=0, keepdims=True)
        peak_ref[k] = peak
        sum_ref[k] = jnp.sum(jnp.exp(scores - peak), axis=0, keepdims=True)
        return carry

    lax.fori_loop(0, lhs_slot.shape[0], one_slot, 0, unroll=4)


def slot_partials(lhs_slot, rhs_slot, lhs, rhs, bias):
    slots = lhs_slot.shape[0]
    blocks, block_size, dim = lhs.shape
    part = jax.ShapeDtypeStruct((slots, 1, rhs.shape[2]), jnp.float32)
    smem = pl.BlockSpec(memory_space=pltpu.SMEM)
    vmem = pl.BlockSpec(memory_space=pltpu.VMEM)
    peak_parts, sum_parts = pl.pallas_call(
        slot_kernel,
        out_shape=(part, part),
        in_specs=[smem, smem, vmem, vmem, vmem],
        out_specs=(vmem, vmem),
        scratch_shapes=[pltpu.VMEM((blocks, block_size, LANES), jnp.float32)],
        cost_estimate=pl.CostEstimate(
            flops=2 * slots * block_size * dim * rhs.shape[2],
            transcendentals=slots * block_size * rhs.shape[2],
            bytes_accessed=(lhs.size + rhs.size) * 2 + 2 * slots * rhs.shape[2] * 4,
        ),
    )(lhs_slot, rhs_slot, lhs, rhs, bias.reshape(blocks, 1, block_size))
    return (peak_parts.reshape(slots, -1), sum_parts.reshape(slots, -1))


def block_combine(peak_parts, sum_parts, members, slot_block, usable):
    block_peak = jnp.max(jnp.where(members[:, :, None], peak_parts[None, :, :], neg_big), axis=1)
    scale = jnp.where(usable[:, None], jnp.exp(peak_parts - block_peak[slot_block]), 0.0)
    block_sum = jnp.dot(
        members.astype(jnp.float32), sum_parts * scale, precision=lax.Precision.HIGHEST
    )
    return (block_peak, block_sum)


def merge_pair(low, high):
    top = jnp.maximum(low[0], high[0])
    total = low[1] * jnp.exp(low[0] - top) + high[1] * jnp.exp(high[0] - top)
    return jnp.stack([top, total])


def round_bits(size, widest):
    bits = size.bit_length() - 1
    plan = []
    first = 0
    while first < bits:
        width = min(widest, bits - first)
        plan.append((first, width))
        first += width
    return plan


def lse_allreduce(peak_vals, totals, axis, widest):
    size = lax.axis_size(axis)
    if size & (size - 1):
        whole_peak = lax.pmax(peak_vals, axis)
        whole_sum = lax.psum(totals * jnp.exp(peak_vals - whole_peak), axis)
        return (whole_peak, whole_sum)
    here = lax.axis_index(axis)
    pair = jnp.stack([peak_vals, totals])
    for first, width in round_bits(size, widest):
        step = 1 << first
        held = {0: pair}
        for offset in range(1, 1 << width):
            shift = offset * step
            held[offset] = lax.ppermute(pair, axis, [(i, i ^ shift) for i in range(size)])
        for level in range(width):
            low_side = (here // (step << level)) % 2 == 0
            merged = {}
            for offset, value in held.items():
                if offset & (1 << level):
                    continue
                other = held[offset | (1 << level)]
                low = jnp.where(low_side, value, other)
                high = jnp.where(low_side, other, value)
                merged[offset] = merge_pair(low, high)
            held = merged
        pair = held[0]
    return (pair[0], pair[1])


def potential_from(peak_vals, totals, log_mass):
    return eps_reg * (log_mass - (peak_vals + jnp.log(totals)))


def body(row_points, col_points, block_lists):
    row_blocks_here = row_points.shape[0]
    col_blocks_here = col_points.shape[0]
    block_size = row_points.shape[2]
    row_mass = -math.log(lax.axis_size("row") * row_blocks_here * block_size)
    col_mass = -math.log(lax.axis_size("col") * col_blocks_here * block_size)
    row_norms = jnp.sum(jnp.square(row_points.astype(jnp.float32)), axis=1)
    col_norms = jnp.sum(jnp.square(col_points.astype(jnp.float32)), axis=1)
    owned = (block_lists // col_blocks_here == lax.axis_index("col")).reshape(-1)
    entry_rank = jnp.cumsum(owned.astype(jnp.int32)) - 1
    slot_list = jnp.arange(CAPACITY, dtype=jnp.int32)
    picked = owned[None, :] & (entry_rank[None, :] == slot_list[:, None])
    entries = jnp.arange(owned.shape[0], dtype=jnp.int32)
    entry_of_slot = jnp.sum(jnp.where(picked, entries[None, :], 0), axis=1)
    usable = jnp.any(picked, axis=1)
    row_slot = entry_of_slot // block_lists.shape[1]
    col_slot = block_lists.reshape(-1)[entry_of_slot] % col_blocks_here
    row_members = (row_slot[None, :] == jnp.arange(row_blocks_here)[:, None]) & usable[None, :]
    col_members = (col_slot[None, :] == jnp.arange(col_blocks_here)[:, None]) & usable[None, :]
    row_t = jnp.swapaxes(row_points, 1, 2)
    col_t = jnp.swapaxes(col_points, 1, 2)
    row_own = -row_norms / (DIM * eps_reg)
    col_own = -col_norms / (DIM * eps_reg)
    def sweep(step, carry):
        row_potential, col_potential = carry
        col_bias = (col_potential - col_norms / DIM) / eps_reg
        peak_parts, sum_parts = slot_partials(
            col_slot, row_slot, col_t, row_points, col_bias
        )
        block_peak, block_sum = block_combine(peak_parts, sum_parts, row_members, row_slot, usable)
        whole_peak, whole_sum = lse_allreduce(block_peak + row_own, block_sum, "col", 2)
        row_potential = potential_from(whole_peak, whole_sum, row_mass)
        row_bias = (row_potential - row_norms / DIM) / eps_reg
        peak_parts, sum_parts = slot_partials(
            row_slot, col_slot, row_t, col_points, row_bias
        )
        block_peak, block_sum = block_combine(peak_parts, sum_parts, col_members, col_slot, usable)
        whole_peak, whole_sum = lse_allreduce(block_peak + col_own, block_sum, "row", 3)
        col_potential = potential_from(whole_peak, whole_sum, col_mass)
        return (row_potential, col_potential)

    start = (
        jnp.zeros((row_blocks_here, block_size), jnp.float32),
        jnp.zeros((col_blocks_here, block_size), jnp.float32),
    )
    row_potential, col_potential = lax.fori_loop(0, ITERS, sweep, start)
    return (row_potential, col_potential)


def solution(mesh):
    placed = (P("row", None, None), P("col", None, None), P("row", None))
    return jax.shard_map(
        body,
        mesh=mesh,
        in_specs=placed,
        out_specs=(P("row", None), P("col", None)),
        check_vma=False,
    )
```

```python
import math

import jax
import jax.numpy as jnp
from jax import lax
from jax.experimental import pallas as pl
from jax.experimental.pallas import tpu as pltpu
from jax.sharding import PartitionSpec as P

DIM = 64
ITERS = 4
CAPACITY = 64
LANES = 128


eps_reg = 0.05
neg_big = -1e30
ip_scale = 2.0 / (DIM * eps_reg)


def slot_kernel(lhs_slot, rhs_slot, lhs_ref, rhs_ref, bias_ref, peak_ref, sum_ref, spread_ref):
    lanes = spread_ref.shape[2]

    def spread(block, carry):
        row = jnp.broadcast_to(bias_ref[block], (lanes, bias_ref.shape[2]))
        spread_ref[block] = jnp.transpose(row)
        return carry

    lax.fori_loop(0, spread_ref.shape[0], spread, 0, unroll=4)

    def one_slot(k, carry):
        a = lhs_slot[k]
        tile = jnp.dot(lhs_ref[a], rhs_ref[rhs_slot[k]], preferred_element_type=jnp.float32)
        bias = spread_ref[a]
        bias = jnp.concatenate([bias] * (tile.shape[1] // lanes), axis=1)
        scores = tile * ip_scale + bias
        peak = jnp.max(scores, axis=0, keepdims=True)
        peak_ref[k] = peak
        sum_ref[k] = jnp.sum(jnp.exp(scores - peak), axis=0, keepdims=True)
        return carry

    lax.fori_loop(0, lhs_slot.shape[0], one_slot, 0, unroll=4)


def slot_partials(lhs_slot, rhs_slot, lhs, rhs, bias):
    slots = lhs_slot.shape[0]
    blocks, block_size, dim = lhs.shape
    part = jax.ShapeDtypeStruct((slots, 1, rhs.shape[2]), jnp.float32)
    smem = pl.BlockSpec(memory_space=pltpu.SMEM)
    vmem = pl.BlockSpec(memory_space=pltpu.VMEM)
    peak_parts, sum_parts = pl.pallas_call(
        slot_kernel,
        out_shape=(part, part),
        in_specs=[smem, smem, vmem, vmem, vmem],
        out_specs=(vmem, vmem),
        scratch_shapes=[pltpu.VMEM((blocks, block_size, LANES), jnp.float32)],
        cost_estimate=pl.CostEstimate(
            flops=2 * slots * block_size * dim * rhs.shape[2],
            transcendentals=slots * block_size * rhs.shape[2],
            bytes_accessed=(lhs.size + rhs.size) * 2 + 2 * slots * rhs.shape[2] * 4,
        ),
    )(lhs_slot, rhs_slot, lhs, rhs, bias.reshape(blocks, 1, block_size))
    return (peak_parts.reshape(slots, -1), sum_parts.reshape(slots, -1))


def block_combine(peak_parts, sum_parts, members, slot_block, usable):
    block_peak = jnp.max(jnp.where(members[:, :, None], peak_parts[None, :, :], neg_big), axis=1)
    scale = jnp.where(usable[:, None], jnp.exp(peak_parts - block_peak[slot_block]), 0.0)
    block_sum = jnp.dot(
        members.astype(jnp.float32), sum_parts * scale, precision=lax.Precision.HIGHEST
    )
    return (block_peak, block_sum)


def merge_pair(low, high):
    top = jnp.maximum(low[0], high[0])
    total = low[1] * jnp.exp(low[0] - top) + high[1] * jnp.exp(high[0] - top)
    return jnp.stack([top, total])


def round_bits(size, widest):
    bits = size.bit_length() - 1
    plan = []
    first = 0
    while first < bits:
        width = min(widest, bits - first)
        plan.append((first, width))
        first += width
    return plan


def lse_allreduce(peak_vals, totals, axis, widest):
    size = lax.axis_size(axis)
    if size & (size - 1):
        whole_peak = lax.pmax(peak_vals, axis)
        whole_sum = lax.psum(totals * jnp.exp(peak_vals - whole_peak), axis)
        return (whole_peak, whole_sum)
    here = lax.axis_index(axis)
    pair = jnp.stack([peak_vals, totals])
    for first, width in round_bits(size, widest):
        step = 1 << first
        held = {0: pair}
        for offset in range(1, 1 << width):
            shift = offset * step
            held[offset] = lax.ppermute(pair, axis, [(i, i ^ shift) for i in range(size)])
        for level in range(width):
            low_side = (here // (step << level)) % 2 == 0
            merged = {}
            for offset, value in held.items():
                if offset & (1 << level):
                    continue
                other = held[offset | (1 << level)]
                low = jnp.where(low_side, value, other)
                high = jnp.where(low_side, other, value)
                merged[offset] = merge_pair(low, high)
            held = merged
        pair = held[0]
    return (pair[0], pair[1])


def lse_exchange(peak_vals, totals, axis):
    size = lax.axis_size(axis)
    blocks = peak_vals.shape[0]
    if blocks % size:
        return lse_allreduce(peak_vals, totals, axis, 2)
    pair = jnp.stack([peak_vals, totals])
    parts = lax.all_to_all(pair, axis, 1, 1, tiled=True)
    parts = parts.reshape(2, size, blocks // size, -1)
    top = jnp.max(parts[0], axis=0)
    total = jnp.sum(parts[1] * jnp.exp(parts[0] - top[None]), axis=0)
    mine = jnp.stack([top, total])
    spread = jnp.broadcast_to(mine[:, None], (2, size) + mine.shape[1:])
    spread = spread.reshape(2, blocks, -1)
    whole = lax.all_to_all(spread, axis, 1, 1, tiled=True)
    return (whole[0], whole[1])


def potential_from(peak_vals, totals, log_mass):
    return eps_reg * (log_mass - (peak_vals + jnp.log(totals)))


def body(row_points, col_points, block_lists):
    row_blocks_here = row_points.shape[0]
    col_blocks_here = col_points.shape[0]
    block_size = row_points.shape[2]
    row_mass = -math.log(lax.axis_size("row") * row_blocks_here * block_size)
    col_mass = -math.log(lax.axis_size("col") * col_blocks_here * block_size)
    row_norms = jnp.sum(jnp.square(row_points.astype(jnp.float32)), axis=1)
    col_norms = jnp.sum(jnp.square(col_points.astype(jnp.float32)), axis=1)
    owned = (block_lists // col_blocks_here == lax.axis_index("col")).reshape(-1)
    entry_rank = jnp.cumsum(owned.astype(jnp.int32)) - 1
    slot_list = jnp.arange(CAPACITY, dtype=jnp.int32)
    picked = owned[None, :] & (entry_rank[None, :] == slot_list[:, None])
    entries = jnp.arange(owned.shape[0], dtype=jnp.int32)
    entry_of_slot = jnp.sum(jnp.where(picked, entries[None, :], 0), axis=1)
    usable = jnp.any(picked, axis=1)
    row_slot = entry_of_slot // block_lists.shape[1]
    col_slot = block_lists.reshape(-1)[entry_of_slot] % col_blocks_here
    row_members = (row_slot[None, :] == jnp.arange(row_blocks_here)[:, None]) & usable[None, :]
    col_members = (col_slot[None, :] == jnp.arange(col_blocks_here)[:, None]) & usable[None, :]
    row_t = jnp.swapaxes(row_points, 1, 2)
    col_t = jnp.swapaxes(col_points, 1, 2)
    row_own = -row_norms / (DIM * eps_reg)
    col_own = -col_norms / (DIM * eps_reg)
    def sweep(step, carry):
        row_potential, col_potential = carry
        col_bias = (col_potential - col_norms / DIM) / eps_reg
        peak_parts, sum_parts = slot_partials(
            col_slot, row_slot, col_t, row_points, col_bias
        )
        block_peak, block_sum = block_combine(peak_parts, sum_parts, row_members, row_slot, usable)
        whole_peak, whole_sum = lse_exchange(block_peak + row_own, block_sum, "col")
        row_potential = potential_from(whole_peak, whole_sum, row_mass)
        row_bias = (row_potential - row_norms / DIM) / eps_reg
        peak_parts, sum_parts = slot_partials(
            row_slot, col_slot, row_t, col_points, row_bias
        )
        block_peak, block_sum = block_combine(peak_parts, sum_parts, col_members, col_slot, usable)
        whole_peak, whole_sum = lse_allreduce(block_peak + col_own, block_sum, "row", 3)
        col_potential = potential_from(whole_peak, whole_sum, col_mass)
        return (row_potential, col_potential)

    start = (
        jnp.zeros((row_blocks_here, block_size), jnp.float32),
        jnp.zeros((col_blocks_here, block_size), jnp.float32),
    )
    row_potential, col_potential = lax.fori_loop(0, ITERS, sweep, start)
    return (row_potential, col_potential)


def solution(mesh):
    placed = (P("row", None, None), P("col", None, None), P("row", None))
    return jax.shard_map(
        body,
        mesh=mesh,
        in_specs=placed,
        out_specs=(P("row", None), P("col", None)),
        check_vma=False,
    )
```

```python
import math

import jax
import jax.numpy as jnp
from jax import lax
from jax.experimental import pallas as pl
from jax.experimental.pallas import tpu as pltpu
from jax.sharding import PartitionSpec as P

DIM = 64
ITERS = 4
CAPACITY = 64
LANES = 128


eps_reg = 0.05
neg_big = -1e30
ip_scale = 2.0 / (DIM * eps_reg)


def slot_kernel(
    lhs_slot, rhs_slot, out_slot, usable, lhs_ref, rhs_ref, bias_ref, peak_ref, sum_ref, spread_ref
):
    lanes = spread_ref.shape[2]

    def spread(block, carry):
        row = jnp.broadcast_to(bias_ref[block], (lanes, bias_ref.shape[2]))
        spread_ref[block] = jnp.transpose(row)
        return carry

    lax.fori_loop(0, spread_ref.shape[0], spread, 0, unroll=4)
    peak_ref[...] = jnp.full(peak_ref.shape, neg_big, jnp.float32)
    sum_ref[...] = jnp.zeros(sum_ref.shape, jnp.float32)

    def one_slot(k, carry):
        a = lhs_slot[k]
        tile = jnp.dot(lhs_ref[a], rhs_ref[rhs_slot[k]], preferred_element_type=jnp.float32)
        bias = spread_ref[a]
        bias = jnp.concatenate([bias] * (tile.shape[1] // lanes), axis=1)
        scores = tile * ip_scale + bias
        peak = jnp.max(scores, axis=0, keepdims=True)
        total = jnp.sum(jnp.exp(scores - peak), axis=0, keepdims=True)
        live = usable[k] > 0
        peak = jnp.where(live, peak, neg_big)
        total = jnp.where(live, total, 0.0)
        b = out_slot[k]
        old_peak = peak_ref[b]
        top = jnp.maximum(old_peak, peak)
        sum_ref[b] = sum_ref[b] * jnp.exp(old_peak - top) + total * jnp.exp(peak - top)
        peak_ref[b] = top
        return carry

    lax.fori_loop(0, lhs_slot.shape[0], one_slot, 0, unroll=8)


def block_partials(lhs_slot, rhs_slot, out_slot, usable, out_blocks, lhs, rhs, bias):
    slots = lhs_slot.shape[0]
    blocks, block_size, dim = lhs.shape
    part = jax.ShapeDtypeStruct((out_blocks, 1, rhs.shape[2]), jnp.float32)
    smem = pl.BlockSpec(memory_space=pltpu.SMEM)
    vmem = pl.BlockSpec(memory_space=pltpu.VMEM)
    block_peak, block_sum = pl.pallas_call(
        slot_kernel,
        out_shape=(part, part),
        in_specs=[smem, smem, smem, smem, vmem, vmem, vmem],
        out_specs=(vmem, vmem),
        scratch_shapes=[pltpu.VMEM((blocks, block_size, LANES), jnp.float32)],
        cost_estimate=pl.CostEstimate(
            flops=2 * slots * block_size * dim * rhs.shape[2],
            transcendentals=slots * block_size * rhs.shape[2],
            bytes_accessed=(lhs.size + rhs.size) * 2 + 2 * out_blocks * rhs.shape[2] * 4,
        ),
    )(lhs_slot, rhs_slot, out_slot, usable, lhs, rhs, bias.reshape(blocks, 1, block_size))
    return (block_peak.reshape(out_blocks, -1), block_sum.reshape(out_blocks, -1))


def merge_pair(low, high):
    top = jnp.maximum(low[0], high[0])
    total = low[1] * jnp.exp(low[0] - top) + high[1] * jnp.exp(high[0] - top)
    return jnp.stack([top, total])


def round_bits(size, widest):
    bits = size.bit_length() - 1
    plan = []
    first = 0
    while first < bits:
        width = min(widest, bits - first)
        plan.append((first, width))
        first += width
    return plan


def lse_allreduce(peak_vals, totals, axis, widest):
    size = lax.axis_size(axis)
    if size & (size - 1):
        whole_peak = lax.pmax(peak_vals, axis)
        whole_sum = lax.psum(totals * jnp.exp(peak_vals - whole_peak), axis)
        return (whole_peak, whole_sum)
    here = lax.axis_index(axis)
    pair = jnp.stack([peak_vals, totals])
    for first, width in round_bits(size, widest):
        step = 1 << first
        held = {0: pair}
        for offset in range(1, 1 << width):
            shift = offset * step
            held[offset] = lax.ppermute(pair, axis, [(i, i ^ shift) for i in range(size)])
        for level in range(width):
            low_side = (here // (step << level)) % 2 == 0
            merged = {}
            for offset, value in held.items():
                if offset & (1 << level):
                    continue
                other = held[offset | (1 << level)]
                low = jnp.where(low_side, value, other)
                high = jnp.where(low_side, other, value)
                merged[offset] = merge_pair(low, high)
            held = merged
        pair = held[0]
    return (pair[0], pair[1])


def lse_exchange(peak_vals, totals, axis):
    size = lax.axis_size(axis)
    blocks = peak_vals.shape[0]
    if blocks % size:
        return lse_allreduce(peak_vals, totals, axis, 2)
    pair = jnp.stack([peak_vals, totals])
    parts = lax.all_to_all(pair, axis, 1, 1, tiled=True)
    parts = parts.reshape(2, size, blocks // size, -1)
    top = jnp.max(parts[0], axis=0)
    total = jnp.sum(parts[1] * jnp.exp(parts[0] - top[None]), axis=0)
    mine = jnp.stack([top, total])
    spread = jnp.broadcast_to(mine[:, None], (2, size) + mine.shape[1:])
    spread = spread.reshape(2, blocks, -1)
    whole = lax.all_to_all(spread, axis, 1, 1, tiled=True)
    return (whole[0], whole[1])


def potential_from(peak_vals, totals, log_mass):
    return eps_reg * (log_mass - (peak_vals + jnp.log(totals)))


def body(row_points, col_points, block_lists):
    row_blocks_here = row_points.shape[0]
    col_blocks_here = col_points.shape[0]
    block_size = row_points.shape[2]
    row_mass = -math.log(lax.axis_size("row") * row_blocks_here * block_size)
    col_mass = -math.log(lax.axis_size("col") * col_blocks_here * block_size)
    row_norms = jnp.sum(jnp.square(row_points.astype(jnp.float32)), axis=1)
    col_norms = jnp.sum(jnp.square(col_points.astype(jnp.float32)), axis=1)
    owned = (block_lists // col_blocks_here == lax.axis_index("col")).reshape(-1)
    entry_rank = jnp.cumsum(owned.astype(jnp.int32)) - 1
    slot_list = jnp.arange(CAPACITY, dtype=jnp.int32)
    picked = owned[None, :] & (entry_rank[None, :] == slot_list[:, None])
    entries = jnp.arange(owned.shape[0], dtype=jnp.int32)
    entry_of_slot = jnp.sum(jnp.where(picked, entries[None, :], 0), axis=1)
    usable = jnp.any(picked, axis=1)
    row_slot = entry_of_slot // block_lists.shape[1]
    col_slot = block_lists.reshape(-1)[entry_of_slot] % col_blocks_here
    live = usable.astype(jnp.int32)
    row_t = jnp.swapaxes(row_points, 1, 2)
    col_t = jnp.swapaxes(col_points, 1, 2)
    row_own = -row_norms / (DIM * eps_reg)
    col_own = -col_norms / (DIM * eps_reg)
    def sweep(step, carry):
        row_potential, col_potential = carry
        col_bias = (col_potential - col_norms / DIM) / eps_reg
        block_peak, block_sum = block_partials(
            col_slot, row_slot, row_slot, live, row_blocks_here, col_t, row_points, col_bias
        )
        whole_peak, whole_sum = lse_exchange(block_peak + row_own, block_sum, "col")
        row_potential = potential_from(whole_peak, whole_sum, row_mass)
        row_bias = (row_potential - row_norms / DIM) / eps_reg
        block_peak, block_sum = block_partials(
            row_slot, col_slot, col_slot, live, col_blocks_here, row_t, col_points, row_bias
        )
        whole_peak, whole_sum = lse_allreduce(block_peak + col_own, block_sum, "row", 3)
        col_potential = potential_from(whole_peak, whole_sum, col_mass)
        return (row_potential, col_potential)

    start = (
        jnp.zeros((row_blocks_here, block_size), jnp.float32),
        jnp.zeros((col_blocks_here, block_size), jnp.float32),
    )
    row_potential, col_potential = lax.fori_loop(0, ITERS, sweep, start)
    return (row_potential, col_potential)


def solution(mesh):
    placed = (P("row", None, None), P("col", None, None), P("row", None))
    return jax.shard_map(
        body,
        mesh=mesh,
        in_specs=placed,
        out_specs=(P("row", None), P("col", None)),
        check_vma=False,
    )
```

```python
import math

import jax
import jax.numpy as jnp
from jax import lax
from jax.experimental import pallas as pl
from jax.experimental.pallas import tpu as pltpu
from jax.sharding import PartitionSpec as P

DIM = 64
ITERS = 4
CAPACITY = 64
LANES = 128


eps_reg = 0.05
neg_big = -1e30
ip_scale = 2.0 / (DIM * eps_reg)


def slot_kernel(
    lhs_slot, rhs_slot, out_slot, usable, lhs_ref, rhs_ref, bias_ref, peak_ref, sum_ref, spread_ref
):
    lanes = spread_ref.shape[2]

    def spread(block, carry):
        row = jnp.broadcast_to(bias_ref[block], (lanes, bias_ref.shape[2]))
        spread_ref[block] = jnp.transpose(row)
        return carry

    lax.fori_loop(0, spread_ref.shape[0], spread, 0, unroll=8)
    peak_ref[...] = jnp.full(peak_ref.shape, neg_big, jnp.float32)
    sum_ref[...] = jnp.zeros(sum_ref.shape, jnp.float32)

    def one_slot(k, carry):
        a = lhs_slot[k]
        tile = jnp.dot(lhs_ref[a], rhs_ref[rhs_slot[k]], preferred_element_type=jnp.float32)
        bias = spread_ref[a]
        bias = jnp.concatenate([bias] * (tile.shape[1] // lanes), axis=1)
        scores = tile * ip_scale + bias
        peak = jnp.max(scores, axis=0, keepdims=True)
        total = jnp.sum(jnp.exp(scores - peak), axis=0, keepdims=True)
        live = usable[k] > 0
        peak = jnp.where(live, peak, neg_big)
        total = jnp.where(live, total, 0.0)
        b = out_slot[k]
        old_peak = peak_ref[b]
        top = jnp.maximum(old_peak, peak)
        sum_ref[b] = sum_ref[b] * jnp.exp(old_peak - top) + total * jnp.exp(peak - top)
        peak_ref[b] = top
        return carry

    lax.fori_loop(0, lhs_slot.shape[0], one_slot, 0, unroll=16)


def block_partials(lhs_slot, rhs_slot, out_slot, usable, out_blocks, lhs, rhs, bias):
    slots = lhs_slot.shape[0]
    blocks, block_size, dim = lhs.shape
    part = jax.ShapeDtypeStruct((out_blocks, 1, rhs.shape[2]), jnp.float32)
    smem = pl.BlockSpec(memory_space=pltpu.SMEM)
    vmem = pl.BlockSpec(memory_space=pltpu.VMEM)
    block_peak, block_sum = pl.pallas_call(
        slot_kernel,
        out_shape=(part, part),
        in_specs=[smem, smem, smem, smem, vmem, vmem, vmem],
        out_specs=(vmem, vmem),
        scratch_shapes=[pltpu.VMEM((blocks, block_size, LANES), jnp.float32)],
        cost_estimate=pl.CostEstimate(
            flops=2 * slots * block_size * dim * rhs.shape[2],
            transcendentals=slots * block_size * rhs.shape[2],
            bytes_accessed=(lhs.size + rhs.size) * 2 + 2 * out_blocks * rhs.shape[2] * 4,
        ),
    )(lhs_slot, rhs_slot, out_slot, usable, lhs, rhs, bias.reshape(blocks, 1, block_size))
    return (block_peak.reshape(out_blocks, -1), block_sum.reshape(out_blocks, -1))


def merge_pair(low, high):
    top = jnp.maximum(low[0], high[0])
    total = low[1] * jnp.exp(low[0] - top) + high[1] * jnp.exp(high[0] - top)
    return jnp.stack([top, total])


def round_bits(size, widest):
    bits = size.bit_length() - 1
    plan = []
    first = 0
    while first < bits:
        width = min(widest, bits - first)
        plan.append((first, width))
        first += width
    return plan


def lse_allreduce(peak_vals, totals, axis, widest):
    size = lax.axis_size(axis)
    if size & (size - 1):
        whole_peak = lax.pmax(peak_vals, axis)
        whole_sum = lax.psum(totals * jnp.exp(peak_vals - whole_peak), axis)
        return (whole_peak, whole_sum)
    here = lax.axis_index(axis)
    pair = jnp.stack([peak_vals, totals])
    for first, width in round_bits(size, widest):
        step = 1 << first
        held = {0: pair}
        for offset in range(1, 1 << width):
            shift = offset * step
            held[offset] = lax.ppermute(pair, axis, [(i, i ^ shift) for i in range(size)])
        for level in range(width):
            low_side = (here // (step << level)) % 2 == 0
            merged = {}
            for offset, value in held.items():
                if offset & (1 << level):
                    continue
                other = held[offset | (1 << level)]
                low = jnp.where(low_side, value, other)
                high = jnp.where(low_side, other, value)
                merged[offset] = merge_pair(low, high)
            held = merged
        pair = held[0]
    return (pair[0], pair[1])


def lse_exchange(peak_vals, totals, axis):
    size = lax.axis_size(axis)
    blocks = peak_vals.shape[0]
    if blocks % size:
        return lse_allreduce(peak_vals, totals, axis, 2)
    pair = jnp.stack([peak_vals, totals])
    parts = lax.all_to_all(pair, axis, 1, 1, tiled=True)
    parts = parts.reshape(2, size, blocks // size, -1)
    top = jnp.max(parts[0], axis=0)
    total = jnp.sum(parts[1] * jnp.exp(parts[0] - top[None]), axis=0)
    mine = jnp.stack([top, total])
    spread = jnp.broadcast_to(mine[:, None], (2, size) + mine.shape[1:])
    spread = spread.reshape(2, blocks, -1)
    whole = lax.all_to_all(spread, axis, 1, 1, tiled=True)
    return (whole[0], whole[1])


def potential_from(peak_vals, totals, log_mass):
    return eps_reg * (log_mass - (peak_vals + jnp.log(totals)))


def body(row_points, col_points, block_lists):
    row_blocks_here = row_points.shape[0]
    col_blocks_here = col_points.shape[0]
    block_size = row_points.shape[2]
    row_mass = -math.log(lax.axis_size("row") * row_blocks_here * block_size)
    col_mass = -math.log(lax.axis_size("col") * col_blocks_here * block_size)
    row_norms = jnp.sum(jnp.square(row_points.astype(jnp.float32)), axis=1)
    col_norms = jnp.sum(jnp.square(col_points.astype(jnp.float32)), axis=1)
    owned = (block_lists // col_blocks_here == lax.axis_index("col")).reshape(-1)
    entry_rank = jnp.cumsum(owned.astype(jnp.int32)) - 1
    slot_list = jnp.arange(CAPACITY, dtype=jnp.int32)
    picked = owned[None, :] & (entry_rank[None, :] == slot_list[:, None])
    entries = jnp.arange(owned.shape[0], dtype=jnp.int32)
    entry_of_slot = jnp.sum(jnp.where(picked, entries[None, :], 0), axis=1)
    usable = jnp.any(picked, axis=1)
    row_slot = entry_of_slot // block_lists.shape[1]
    col_slot = block_lists.reshape(-1)[entry_of_slot] % col_blocks_here
    live = usable.astype(jnp.int32)
    row_t = jnp.swapaxes(row_points, 1, 2)
    col_t = jnp.swapaxes(col_points, 1, 2)
    row_own = -row_norms / (DIM * eps_reg)
    col_own = -col_norms / (DIM * eps_reg)
    def sweep(step, carry):
        row_potential, col_potential = carry
        col_bias = (col_potential - col_norms / DIM) / eps_reg
        block_peak, block_sum = block_partials(
            col_slot, row_slot, row_slot, live, row_blocks_here, col_t, row_points, col_bias
        )
        whole_peak, whole_sum = lse_exchange(block_peak + row_own, block_sum, "col")
        row_potential = potential_from(whole_peak, whole_sum, row_mass)
        row_bias = (row_potential - row_norms / DIM) / eps_reg
        block_peak, block_sum = block_partials(
            row_slot, col_slot, col_slot, live, col_blocks_here, row_t, col_points, row_bias
        )
        whole_peak, whole_sum = lse_allreduce(block_peak + col_own, block_sum, "row", 3)
        col_potential = potential_from(whole_peak, whole_sum, col_mass)
        return (row_potential, col_potential)

    start = (
        jnp.zeros((row_blocks_here, block_size), jnp.float32),
        jnp.zeros((col_blocks_here, block_size), jnp.float32),
    )
    row_potential, col_potential = lax.fori_loop(0, ITERS, sweep, start)
    return (row_potential, col_potential)


def solution(mesh):
    placed = (P("row", None, None), P("col", None, None), P("row", None))
    return jax.shard_map(
        body,
        mesh=mesh,
        in_specs=placed,
        out_specs=(P("row", None), P("col", None)),
        check_vma=False,
    )
```

```python
import math

import jax
import jax.numpy as jnp
from jax import lax
from jax.experimental import pallas as pl
from jax.experimental.pallas import tpu as pltpu
from jax.sharding import PartitionSpec as P

DIM = 64
ITERS = 4
CAPACITY = 64
LANES = 128


eps_reg = 0.05
neg_big = -1e30
ip_scale = 2.0 / (DIM * eps_reg)


def slot_kernel(
    lhs_slot, rhs_slot, out_slot, usable, lhs_ref, rhs_ref, bias_ref, peak_ref, sum_ref, spread_ref
):
    lanes = spread_ref.shape[2]

    def spread(block, carry):
        row = jnp.broadcast_to(bias_ref[block], (lanes, bias_ref.shape[2]))
        spread_ref[block] = jnp.transpose(row)
        return carry

    lax.fori_loop(0, spread_ref.shape[0], spread, 0, unroll=8)
    peak_ref[...] = jnp.full(peak_ref.shape, neg_big, jnp.float32)
    sum_ref[...] = jnp.zeros(sum_ref.shape, jnp.float32)

    def one_slot(k, carry):
        a = lhs_slot[k]
        tile = jnp.dot(lhs_ref[a], rhs_ref[rhs_slot[k]], preferred_element_type=jnp.float32)
        bias = spread_ref[a]
        bias = jnp.concatenate([bias] * (tile.shape[1] // lanes), axis=1)
        scores = tile * ip_scale + bias
        peak = jnp.max(scores, axis=0, keepdims=True)
        total = jnp.sum(jnp.exp(scores - peak), axis=0, keepdims=True)
        live = usable[k] > 0
        peak = jnp.where(live, peak, neg_big)
        total = jnp.where(live, total, 0.0)
        b = out_slot[k]
        old_peak = peak_ref[b]
        top = jnp.maximum(old_peak, peak)
        sum_ref[b] = sum_ref[b] * jnp.exp(old_peak - top) + total * jnp.exp(peak - top)
        peak_ref[b] = top
        return carry

    lax.fori_loop(0, lhs_slot.shape[0], one_slot, 0, unroll=16)


def block_partials(lhs_slot, rhs_slot, out_slot, usable, out_blocks, lhs, rhs, bias):
    slots = lhs_slot.shape[0]
    blocks, block_size, dim = lhs.shape
    part = jax.ShapeDtypeStruct((out_blocks, 1, rhs.shape[2]), jnp.float32)
    smem = pl.BlockSpec(memory_space=pltpu.SMEM)
    vmem = pl.BlockSpec(memory_space=pltpu.VMEM)
    block_peak, block_sum = pl.pallas_call(
        slot_kernel,
        out_shape=(part, part),
        in_specs=[smem, smem, smem, smem, vmem, vmem, vmem],
        out_specs=(vmem, vmem),
        scratch_shapes=[pltpu.VMEM((blocks, block_size, LANES), jnp.float32)],
        cost_estimate=pl.CostEstimate(
            flops=2 * slots * block_size * dim * rhs.shape[2],
            transcendentals=slots * block_size * rhs.shape[2],
            bytes_accessed=(lhs.size + rhs.size) * 2 + 2 * out_blocks * rhs.shape[2] * 4,
        ),
    )(lhs_slot, rhs_slot, out_slot, usable, lhs, rhs, bias.reshape(blocks, 1, block_size))
    return (block_peak.reshape(out_blocks, -1), block_sum.reshape(out_blocks, -1))


def merge_pair(low, high):
    top = jnp.maximum(low[0], high[0])
    total = low[1] * jnp.exp(low[0] - top) + high[1] * jnp.exp(high[0] - top)
    return jnp.stack([top, total])


def round_bits(size, widest):
    bits = size.bit_length() - 1
    plan = []
    first = 0
    while first < bits:
        width = min(widest, bits - first)
        plan.append((first, width))
        first += width
    return plan


def lse_allreduce(peak_vals, totals, axis, widest):
    size = lax.axis_size(axis)
    if size & (size - 1):
        whole_peak = lax.pmax(peak_vals, axis)
        whole_sum = lax.psum(totals * jnp.exp(peak_vals - whole_peak), axis)
        return (whole_peak, whole_sum)
    here = lax.axis_index(axis)
    pair = jnp.stack([peak_vals, totals])
    for first, width in round_bits(size, widest):
        step = 1 << first
        held = {0: pair}
        for offset in range(1, 1 << width):
            shift = offset * step
            held[offset] = lax.ppermute(pair, axis, [(i, i ^ shift) for i in range(size)])
        for level in range(width):
            low_side = (here // (step << level)) % 2 == 0
            merged = {}
            for offset, value in held.items():
                if offset & (1 << level):
                    continue
                other = held[offset | (1 << level)]
                low = jnp.where(low_side, value, other)
                high = jnp.where(low_side, other, value)
                merged[offset] = merge_pair(low, high)
            held = merged
        pair = held[0]
    return (pair[0], pair[1])


def lse_exchange(peak_vals, totals, axis):
    size = lax.axis_size(axis)
    blocks = peak_vals.shape[0]
    pair = jnp.stack([peak_vals, totals])
    if blocks % size:
        if pair[0].size % (size * LANES):
            return lse_allreduce(peak_vals, totals, axis, 3)
        pair = pair.reshape(2, -1)
    parts = lax.all_to_all(pair, axis, 1, 1, tiled=True)
    parts = parts.reshape((2, size, pair.shape[1] // size) + pair.shape[2:])
    top = jnp.max(parts[0], axis=0)
    total = jnp.sum(parts[1] * jnp.exp(parts[0] - top[None]), axis=0)
    mine = jnp.stack([top, total])
    spread = jnp.broadcast_to(mine[:, None], (2, size) + mine.shape[1:])
    spread = spread.reshape(pair.shape)
    whole = lax.all_to_all(spread, axis, 1, 1, tiled=True)
    whole = whole.reshape((2,) + peak_vals.shape)
    return (whole[0], whole[1])


def potential_from(peak_vals, totals, log_mass):
    return eps_reg * (log_mass - (peak_vals + jnp.log(totals)))


def body(row_points, col_points, block_lists):
    row_blocks_here = row_points.shape[0]
    col_blocks_here = col_points.shape[0]
    block_size = row_points.shape[2]
    row_mass = -math.log(lax.axis_size("row") * row_blocks_here * block_size)
    col_mass = -math.log(lax.axis_size("col") * col_blocks_here * block_size)
    row_norms = jnp.sum(jnp.square(row_points.astype(jnp.float32)), axis=1)
    col_norms = jnp.sum(jnp.square(col_points.astype(jnp.float32)), axis=1)
    owned = (block_lists // col_blocks_here == lax.axis_index("col")).reshape(-1)
    entry_rank = jnp.cumsum(owned.astype(jnp.int32)) - 1
    slot_list = jnp.arange(CAPACITY, dtype=jnp.int32)
    picked = owned[None, :] & (entry_rank[None, :] == slot_list[:, None])
    entries = jnp.arange(owned.shape[0], dtype=jnp.int32)
    entry_of_slot = jnp.sum(jnp.where(picked, entries[None, :], 0), axis=1)
    usable = jnp.any(picked, axis=1)
    row_slot = entry_of_slot // block_lists.shape[1]
    col_slot = block_lists.reshape(-1)[entry_of_slot] % col_blocks_here
    live = usable.astype(jnp.int32)
    row_t = jnp.swapaxes(row_points, 1, 2)
    col_t = jnp.swapaxes(col_points, 1, 2)
    row_own = -row_norms / (DIM * eps_reg)
    col_own = -col_norms / (DIM * eps_reg)
    def sweep(step, carry):
        row_potential, col_potential = carry
        col_bias = (col_potential - col_norms / DIM) / eps_reg
        block_peak, block_sum = block_partials(
            col_slot, row_slot, row_slot, live, row_blocks_here, col_t, row_points, col_bias
        )
        whole_peak, whole_sum = lse_exchange(block_peak + row_own, block_sum, "col")
        row_potential = potential_from(whole_peak, whole_sum, row_mass)
        row_bias = (row_potential - row_norms / DIM) / eps_reg
        block_peak, block_sum = block_partials(
            row_slot, col_slot, col_slot, live, col_blocks_here, row_t, col_points, row_bias
        )
        whole_peak, whole_sum = lse_exchange(block_peak + col_own, block_sum, "row")
        col_potential = potential_from(whole_peak, whole_sum, col_mass)
        return (row_potential, col_potential)

    start = (
        jnp.zeros((row_blocks_here, block_size), jnp.float32),
        jnp.zeros((col_blocks_here, block_size), jnp.float32),
    )
    row_potential, col_potential = lax.fori_loop(0, ITERS, sweep, start)
    return (row_potential, col_potential)


def solution(mesh):
    placed = (P("row", None, None), P("col", None, None), P("row", None))
    return jax.shard_map(
        body,
        mesh=mesh,
        in_specs=placed,
        out_specs=(P("row", None), P("col", None)),
        check_vma=False,
    )
```
